32 devices in a mesh: groups: 2 (over y), range: 8 (over z, x), chan: 2 (over core).
Axes of the slice: x: 2, y: 2, z: 4, core: 2. Of those that a mesh axis runs over, the one named last changes fastest.
Arguments:
- echoes: bfloat16 [4, 512, 8, 1024], P('groups', 'chan', None, 'range'), parts along dimension 0, may hold values from -6 to 6
- chirp: float32 [2, 2049], replicated, may hold values from -0.09375 to 0.09375
- gates: int32 [4, 8], P('groups'), parts along dimension 0, may hold values from 0 to 1023, as said below
Outputs:
- compressed: bfloat16 [4, 512, 8, 1024], P('groups', 'chan', None, 'range'), parts along dimension 0
- covariance: float32 [4, 2, 2048, 4096], P('groups', 'chan', 'range'), parts along dimension 0
The draws below stay inside these ranges and needn't reach their ends.
There are 2 independent parts, one for each index of `groups`. The reference program is written for one: setup_inputs(seed, part) draws one part's arguments, and reference() takes and returns one part's arrays. A program takes and returns all parts, laid end to end along the dimension named above; an argument that names none is the same for every part. Nothing has to cross between parts.
Inputs may be any that keep to these rules, and one draw needn't show every extreme that they name: `gates`: the 8 intervals are given in increasing order, do not intersect, lie within the 1024 cells, each holds one cell or more, and their lengths add up to 128. The first interval starts at cell 0, and the last is the single cell 1024 - 1.
All inputs are finite; a program needn't handle non-finite values.
Results may differ from the reference program's by a relative error of at most 0.0035.
Values may be sent and summed in bfloat16 or wider, within the bound.
No kernel may reach another device: no remote copies, remote signals or barrier semaphores. Data moves between devices by JAX's collectives and lax.ppermute only.
A program may use at most 128 MiB of HBM per device.

```python
import jax
import jax.numpy as jnp
from jax import lax

CH = 512
PULSES = 8
TAPS = 2049
TRAIN = 128
NGATE = 8
RANGE = 1024
ORDER = 4096
N_CHAN = 2


def draw_gates(key, part):
    first_key, second_key = jax.random.split(jax.random.fold_in(key, 17))
    shuffled = jax.random.permutation(first_key, TRAIN - 2) + 1
    cuts = jnp.sort(shuffled[:NGATE - 2])
    bounds = jnp.concatenate([jnp.zeros((1,), jnp.int32), cuts.astype(jnp.int32), jnp.full((1,), TRAIN - 1, jnp.int32)])
    front_widths = bounds[1:] - bounds[:-1]
    widths = jnp.concatenate([front_widths, jnp.ones((1,), jnp.int32)])
    drawn = jnp.sort(jax.random.randint(second_key, (NGATE,), 0, RANGE - TRAIN + 1)).astype(jnp.int32)
    positions = jnp.arange(NGATE, dtype=jnp.int32)
    spaces = jnp.where(positions == 0, 0, jnp.where(positions == NGATE - 1, RANGE - TRAIN, drawn)).astype(jnp.int32)
    before = jnp.concatenate([jnp.zeros((1,), jnp.int32), jnp.cumsum(widths)[:-1].astype(jnp.int32)])
    starts = spaces + before
    return jnp.stack([starts, widths]).astype(jnp.int32)


def block_scale(key, extent, cuts, low, high):
    level, own = 1.0, jax.random.fold_in(key, 6)
    for position, shards_of in cuts:
        draws = jnp.exp(jax.random.uniform(jax.random.fold_in(own, position), (shards_of,), jnp.float32, low / len(cuts), high / len(cuts)))
        level = level * jnp.repeat(draws, extent[position] // shards_of).reshape([-1 if axis == position else 1 for axis in range(len(extent))])
    return level


def scatter_about(own_key, dims, spread, reach, cuts=(), kind=jnp.bfloat16):
    factor_of = block_scale(own_key, dims, cuts, -0.22, 0.18) if cuts else 1.0
    values = jax.random.normal(own_key, dims, jnp.float32) * spread * factor_of
    return jnp.minimum(jnp.maximum(values, -reach), reach).astype(kind)


def setup_inputs(seed: int = 0, part: int = 0) -> dict:
    key_of = jax.random.split(jax.random.key(seed), 4)
    part_keys = jax.random.split(jax.random.fold_in(key_of[3], part), 4)
    echoes = scatter_about(part_keys[0], (2, CH, PULSES, RANGE), 1.0, 6.0, ((1, 2), (3, 8)))
    chirp = scatter_about(key_of[1], (2, TAPS), (2 * TAPS) ** -0.5, 0.09375, (), jnp.float32)
    gates = draw_gates(jax.random.fold_in(jax.random.fold_in(key_of[3], part), 71), part)
    return dict(echoes=echoes, chirp=chirp, gates=gates)


def train_cells(gates, count):
    starts = gates[0]
    widths = gates[1]
    ends = jnp.cumsum(widths)
    places = jnp.arange(count, dtype=jnp.int32)
    which = jnp.sum((ends[None, :] <= places[:, None]).astype(jnp.int32), axis=1)
    onehot = jnp.arange(gates.shape[1], dtype=jnp.int32)[None, :] == which[:, None]
    offset = jnp.sum(jnp.where(onehot, (starts - (ends - widths))[None, :], 0), axis=1)
    return (offset + places).astype(jnp.int32)


def reference(echoes, chirp, gates):
    total = echoes.shape[3]
    length = 1 << (total + TAPS - 2).bit_length()
    spectrum = jnp.fft.fft(lax.complex(chirp[0], chirp[1]), length)

    def filter_channel(channel):
        values = channel.astype(chirp.dtype)
        signal = lax.complex(values[0], values[1])
        result = jnp.fft.ifft(jnp.fft.fft(signal, length, axis=-1) * spectrum[None, :], axis=-1)[:, :total]
        return jnp.stack([jnp.real(result), jnp.imag(result)]).astype(jnp.bfloat16)

    filtered = lax.map(filter_channel, jnp.moveaxis(echoes, 1, 0))
    compressed = jnp.moveaxis(filtered, 0, 1)
    cells = train_cells(gates, TRAIN)
    snapshots = jnp.take(compressed, cells, axis=3).reshape(2, ORDER, TRAIN)
    snap_re = snapshots[0]
    snap_im = snapshots[1]

    def gram(left, right):
        return jnp.dot(left, right.T, preferred_element_type=jnp.float32)

    real_part = gram(snap_re, snap_re) + gram(snap_im, snap_im)
    imag_part = gram(snap_im, snap_re) - gram(snap_re, snap_im)
    full = jnp.stack([real_part, imag_part]) / TRAIN
    covariance = full.reshape(2, N_CHAN, ORDER // N_CHAN, ORDER)
    return compressed, covariance
```

```python
from functools import partial

import jax
import jax.numpy as jnp
from jax import lax
from jax.experimental import pallas as pl
from jax.experimental.pallas import tpu as pltpu
from jax.sharding import PartitionSpec as P

TRAIN = 128
BLOCK = 128


def train_cells(gates, count):
    starts = gates[0]
    widths = gates[1]
    ends = jnp.cumsum(widths)
    places = jnp.arange(count, dtype=jnp.int32)
    which = jnp.sum((ends[None, :] <= places[:, None]).astype(jnp.int32), axis=1)
    onehot = jnp.arange(gates.shape[1], dtype=jnp.int32)[None, :] == which[:, None]
    offset = jnp.sum(jnp.where(onehot, (starts - (ends - widths))[None, :], 0), axis=1)
    return offset + places


def toeplitz_blocks(chirp, lags):
    taps = chirp.shape[1]
    length = BLOCK * lags + BLOCK - 1
    pad_after = max(0, length - (BLOCK - 1) - taps)
    u = jnp.pad(chirp, ((0, 0), (BLOCK - 1, pad_after)))[:, :length]
    tiled = jnp.tile(u, (1, BLOCK + 1))[:, : BLOCK * (length + 1)]
    windows = tiled.reshape(2, BLOCK, length + 1)[:, :, : BLOCK * lags]
    full = windows[:, ::-1, :]
    blocks = full.reshape(2, BLOCK, lags, BLOCK).transpose(0, 2, 1, 3)
    t_re = blocks[0]
    t_im = blocks[1]
    top = jnp.concatenate([t_re, t_im], axis=2)
    bottom = jnp.concatenate([-t_im, t_re], axis=2)
    w = jnp.concatenate([top, bottom], axis=1)
    hi = w.astype(jnp.bfloat16)
    lo = (w - hi.astype(jnp.float32)).astype(jnp.bfloat16)
    return jnp.concatenate([hi, lo], axis=2)


def conv_kernel(x_ref, w_ref, o_ref, *, lags):
    d = pl.program_id(0)
    rows = x_ref.shape[0]
    width = 2 * BLOCK

    def body(j, acc):
        start = pl.multiple_of((d - j) * width, width)
        xs = x_ref[:, pl.ds(start, width)]
        return acc + jnp.dot(xs, w_ref[j], preferred_element_type=jnp.float32)

    count = jnp.minimum(d, lags - 1) + 1
    acc = lax.fori_loop(0, count, body, jnp.zeros((rows, 2 * width), jnp.float32))
    o_ref[...] = (acc[:, :width] + acc[:, width:]).astype(o_ref.dtype)


def causal_filter(x, w):
    rows, total = x.shape
    lags = w.shape[0]
    nblocks = total // (2 * BLOCK)
    work = rows * (2 * BLOCK) * (4 * BLOCK) * 2 * nblocks * min(lags, nblocks)
    return pl.pallas_call(
        partial(conv_kernel, lags=lags),
        out_shape=jax.ShapeDtypeStruct((rows, total), jnp.bfloat16),
        grid=(nblocks,),
        in_specs=[
            pl.BlockSpec((rows, total), lambda d: (0, 0)),
            pl.BlockSpec(w.shape, lambda d: (0, 0, 0)),
        ],
        out_specs=pl.BlockSpec((rows, 2 * BLOCK), lambda d: (0, d)),
        compiler_params=pltpu.CompilerParams(vmem_limit_bytes=48 * 1024 * 1024),
        cost_estimate=pl.CostEstimate(
            flops=work, transcendentals=0, bytes_accessed=2 * x.size * 2 + w.size * 2
        ),
    )(x, w)


def on_device(echoes, chirp, gates):
    chans = echoes.shape[1]
    pulses = echoes.shape[2]
    cells_dev = echoes.shape[3]
    taps = chirp.shape[1]
    ranks = lax.axis_size("range")
    range_len = cells_dev * ranks
    nblocks = range_len // BLOCK
    per_dev_blocks = cells_dev // BLOCK
    lags = min((taps - 1 + BLOCK - 1) // BLOCK + 1, nblocks)
    series_total = chans * pulses
    series_dev = series_total // ranks

    w = toeplitz_blocks(chirp, lags)

    local = echoes.reshape(2, series_total, per_dev_blocks, BLOCK).transpose(1, 2, 0, 3)
    series_all = lax.all_to_all(local, "range", split_axis=0, concat_axis=1, tiled=True)
    x = series_all.reshape(series_dev, nblocks * 2 * BLOCK)
    y = causal_filter(x, w)
    y4 = y.reshape(series_dev, nblocks, 2, BLOCK)

    returned = lax.all_to_all(y4, "range", split_axis=1, concat_axis=0, tiled=True)
    compressed = returned.reshape(chans, pulses, per_dev_blocks, 2, BLOCK)
    compressed = compressed.transpose(3, 0, 1, 2, 4).reshape(2, chans, pulses, cells_dev)

    cells = train_cells(gates, TRAIN)
    by_cell = y4.transpose(1, 3, 0, 2).reshape(range_len, series_dev, 2)
    picked = jnp.take(by_cell, cells, axis=0)
    snap = picked.transpose(1, 2, 0).reshape(series_dev, 2 * TRAIN)

    half = lax.all_gather(snap, "range", axis=0, tiled=True)
    every = lax.all_gather(half, "chan", axis=0, tiled=True)

    snap_re = snap[:, :TRAIN]
    snap_im = snap[:, TRAIN:]
    left = jnp.concatenate([snap, jnp.concatenate([snap_im, -snap_re], axis=1)], axis=0)
    gram = lax.dot_general(
        left, every, (((1,), (1,)), ((), ())), preferred_element_type=jnp.float32
    )
    covariance = (gram * (1.0 / TRAIN)).reshape(2, 1, series_dev, -1)
    return (compressed, covariance)


def solution(mesh):
    placed = (P("groups", "chan", None, "range"), P(), P("groups", None))
    return jax.shard_map(
        on_device,
        mesh=mesh,
        in_specs=placed,
        out_specs=(P("groups", "chan", None, "range"), P("groups", "chan", "range", None)),
        check_vma=False,
    )
```

```python
from functools import partial

import jax
import jax.numpy as jnp
from jax import lax
from jax.experimental import pallas as pl
from jax.experimental.pallas import tpu as pltpu
from jax.sharding import PartitionSpec as P

TRAIN = 128
BLOCK = 128


def train_cells(gates, count):
    starts = gates[0]
    widths = gates[1]
    ends = jnp.cumsum(widths)
    places = jnp.arange(count, dtype=jnp.int32)
    which = jnp.sum((ends[None, :] <= places[:, None]).astype(jnp.int32), axis=1)
    onehot = jnp.arange(gates.shape[1], dtype=jnp.int32)[None, :] == which[:, None]
    offset = jnp.sum(jnp.where(onehot, (starts - (ends - widths))[None, :], 0), axis=1)
    return offset + places


def toeplitz_blocks(chirp, lags):
    taps = chirp.shape[1]
    length = BLOCK * lags + BLOCK - 1
    pad_after = max(0, length - (BLOCK - 1) - taps)
    u = jnp.pad(chirp, ((0, 0), (BLOCK - 1, pad_after)))[:, :length]
    tiled = jnp.tile(u, (1, BLOCK + 1))[:, : BLOCK * (length + 1)]
    windows = tiled.reshape(2, BLOCK, length + 1)[:, :, : BLOCK * lags]
    full = windows[:, ::-1, :]
    blocks = full.reshape(2, BLOCK, lags, BLOCK).transpose(0, 2, 1, 3)
    t_re = blocks[0]
    t_im = blocks[1]
    top = jnp.concatenate([t_re, t_im], axis=2)
    bottom = jnp.concatenate([-t_im, t_re], axis=2)
    w = jnp.concatenate([top, bottom], axis=1)
    hi = w.astype(jnp.bfloat16)
    lo = (w - hi.astype(jnp.float32)).astype(jnp.bfloat16)
    return jnp.concatenate([hi, lo], axis=2)


def conv_kernel(x_ref, w_ref, o_ref, *, lags):
    d = pl.program_id(0)
    rows = x_ref.shape[0]
    width = 2 * BLOCK

    def body(j, acc):
        start = pl.multiple_of((d - j) * width, width)
        xs = x_ref[:, pl.ds(start, width)]
        return acc + jnp.dot(xs, w_ref[j], preferred_element_type=jnp.float32)

    count = jnp.minimum(d, lags - 1) + 1
    acc = lax.fori_loop(0, count, body, jnp.zeros((rows, 2 * width), jnp.float32))
    o_ref[...] = (acc[:, :width] + acc[:, width:]).astype(o_ref.dtype)


def causal_filter(x, w):
    rows, total = x.shape
    lags = w.shape[0]
    nblocks = total // (2 * BLOCK)
    work = rows * (2 * BLOCK) * (4 * BLOCK) * 2 * nblocks * min(lags, nblocks)
    return pl.pallas_call(
        partial(conv_kernel, lags=lags),
        out_shape=jax.ShapeDtypeStruct((rows, total), jnp.bfloat16),
        grid=(nblocks,),
        in_specs=[
            pl.BlockSpec((rows, total), lambda d: (0, 0)),
            pl.BlockSpec(w.shape, lambda d: (0, 0, 0)),
        ],
        out_specs=pl.BlockSpec((rows, 2 * BLOCK), lambda d: (0, d)),
        compiler_params=pltpu.CompilerParams(vmem_limit_bytes=48 * 1024 * 1024),
        cost_estimate=pl.CostEstimate(
            flops=work, transcendentals=0, bytes_accessed=2 * x.size * 2 + w.size * 2
        ),
    )(x, w)


def on_device(echoes, chirp, gates):
    chans = echoes.shape[1]
    pulses = echoes.shape[2]
    cells_dev = echoes.shape[3]
    taps = chirp.shape[1]
    ranks = lax.axis_size("range")
    range_len = cells_dev * ranks
    nblocks = range_len // BLOCK
    per_dev_blocks = cells_dev // BLOCK
    lags = min((taps - 1 + BLOCK - 1) // BLOCK + 1, nblocks)
    series_total = chans * pulses
    series_dev = series_total // ranks

    w = toeplitz_blocks(chirp, lags)

    local = echoes.reshape(2, series_total, per_dev_blocks, BLOCK).transpose(1, 2, 0, 3)
    series_all = lax.all_to_all(local, "range", split_axis=0, concat_axis=1, tiled=True)
    x = series_all.reshape(series_dev, nblocks * 2 * BLOCK)
    y = causal_filter(x, w)
    y4 = y.reshape(series_dev, nblocks, 2, BLOCK)

    cells = train_cells(gates, TRAIN)
    by_cell = y4.transpose(1, 3, 0, 2).reshape(range_len, series_dev, 2)
    picked = jnp.take(by_cell, cells, axis=0)
    snap = picked.transpose(1, 2, 0).reshape(series_dev, 2 * TRAIN)

    own_width = per_dev_blocks * 2 * BLOCK
    spread = jnp.broadcast_to(snap[:, None, :], (series_dev, ranks, 2 * TRAIN))
    both = jnp.concatenate([y.reshape(series_dev, ranks, own_width), spread], axis=2)
    arrived = lax.all_to_all(both, "range", split_axis=1, concat_axis=0, tiled=True)
    returned = arrived[:, 0, :own_width]
    half = arrived[:, 0, own_width:]
    compressed = returned.reshape(chans, pulses, per_dev_blocks, 2, BLOCK)
    compressed = compressed.transpose(3, 0, 1, 2, 4).reshape(2, chans, pulses, cells_dev)

    every = lax.all_gather(half, "chan", axis=0, tiled=True)

    snap_re = snap[:, :TRAIN]
    snap_im = snap[:, TRAIN:]
    left = jnp.concatenate([snap, jnp.concatenate([snap_im, -snap_re], axis=1)], axis=0)
    gram = lax.dot_general(
        left, every, (((1,), (1,)), ((), ())), preferred_element_type=jnp.float32
    )
    covariance = (gram * (1.0 / TRAIN)).reshape(2, 1, series_dev, -1)
    return (compressed, covariance)


def solution(mesh):
    placed = (P("groups", "chan", None, "range"), P(), P("groups", None))
    return jax.shard_map(
        on_device,
        mesh=mesh,
        in_specs=placed,
        out_specs=(P("groups", "chan", None, "range"), P("groups", "chan", "range", None)),
        check_vma=False,
    )
```

```python
from functools import partial

import jax
import jax.numpy as jnp
from jax import lax
from jax.experimental import pallas as pl
from jax.experimental.pallas import tpu as pltpu
from jax.sharding import PartitionSpec as P

TRAIN = 128
BLOCK = 128


def train_cells(gates, count):
    starts = gates[0]
    widths = gates[1]
    ends = jnp.cumsum(widths)
    places = jnp.arange(count, dtype=jnp.int32)
    which = jnp.sum((ends[None, :] <= places[:, None]).astype(jnp.int32), axis=1)
    onehot = jnp.arange(gates.shape[1], dtype=jnp.int32)[None, :] == which[:, None]
    offset = jnp.sum(jnp.where(onehot, (starts - (ends - widths))[None, :], 0), axis=1)
    return offset + places


def toeplitz_blocks(chirp, lags):
    taps = chirp.shape[1]
    length = BLOCK * lags + BLOCK - 1
    pad_after = max(0, length - (BLOCK - 1) - taps)
    u = jnp.pad(chirp, ((0, 0), (BLOCK - 1, pad_after)))[:, :length]
    tiled = jnp.tile(u, (1, BLOCK + 1))[:, : BLOCK * (length + 1)]
    windows = tiled.reshape(2, BLOCK, length + 1)[:, :, : BLOCK * lags]
    full = windows[:, ::-1, :]
    blocks = full.reshape(2, BLOCK, lags, BLOCK).transpose(0, 2, 1, 3)
    t_re = blocks[0]
    t_im = blocks[1]
    top = jnp.concatenate([t_re, t_im], axis=2)
    bottom = jnp.concatenate([-t_im, t_re], axis=2)
    w = jnp.concatenate([top, bottom], axis=1)
    hi = w.astype(jnp.bfloat16)
    lo = (w - hi.astype(jnp.float32)).astype(jnp.bfloat16)
    return jnp.concatenate([hi, lo], axis=2)


def conv_kernel(x_ref, w_ref, o_ref, *, lags):
    d = pl.program_id(0)
    width = 2 * BLOCK
    start = pl.multiple_of(d * width, width)
    xs = x_ref[:, pl.ds(start, lags * width)]
    acc = jnp.dot(xs, w_ref[...], preferred_element_type=jnp.float32)
    o_ref[...] = (acc[:, :width] + acc[:, width:]).astype(o_ref.dtype)


def causal_filter(x, w):
    rows, total = x.shape
    lags = w.shape[0]
    width = 2 * BLOCK
    nblocks = total // width
    stacked = w[::-1].reshape(lags * width, 2 * width)
    padded = jnp.pad(x, ((0, 0), ((lags - 1) * width, 0)))
    work = rows * lags * width * 2 * width * 2 * nblocks
    return pl.pallas_call(
        partial(conv_kernel, lags=lags),
        out_shape=jax.ShapeDtypeStruct((rows, total), jnp.bfloat16),
        grid=(nblocks,),
        in_specs=[
            pl.BlockSpec(padded.shape, lambda d: (0, 0)),
            pl.BlockSpec(stacked.shape, lambda d: (0, 0)),
        ],
        out_specs=pl.BlockSpec((rows, width), lambda d: (0, d)),
        compiler_params=pltpu.CompilerParams(vmem_limit_bytes=48 * 1024 * 1024),
        cost_estimate=pl.CostEstimate(
            flops=work, transcendentals=0, bytes_accessed=2 * x.size * 2 + w.size * 2
        ),
    )(padded, stacked)


def on_device(echoes, chirp, gates):
    chans = echoes.shape[1]
    pulses = echoes.shape[2]
    cells_dev = echoes.shape[3]
    taps = chirp.shape[1]
    ranks = lax.axis_size("range")
    range_len = cells_dev * ranks
    nblocks = range_len // BLOCK
    per_dev_blocks = cells_dev // BLOCK
    lags = min((taps - 1 + BLOCK - 1) // BLOCK + 1, nblocks)
    series_total = chans * pulses
    series_dev = series_total // ranks

    w = toeplitz_blocks(chirp, lags)

    local = echoes.reshape(2, series_total, per_dev_blocks, BLOCK).transpose(1, 2, 0, 3)
    series_all = lax.all_to_all(local, "range", split_axis=0, concat_axis=1, tiled=True)
    x = series_all.reshape(series_dev, nblocks * 2 * BLOCK)
    y = causal_filter(x, w)
    y4 = y.reshape(series_dev, nblocks, 2, BLOCK)

    cells = train_cells(gates, TRAIN)
    by_cell = y4.transpose(1, 3, 0, 2).reshape(range_len, series_dev, 2)
    picked = jnp.take(by_cell, cells, axis=0)
    snap = picked.transpose(1, 2, 0).reshape(series_dev, 2 * TRAIN)

    own_width = per_dev_blocks * 2 * BLOCK
    spread = jnp.broadcast_to(snap[:, None, :], (series_dev, ranks, 2 * TRAIN))
    both = jnp.concatenate([y.reshape(series_dev, ranks, own_width), spread], axis=2)
    arrived = lax.all_to_all(both, "range", split_axis=1, concat_axis=0, tiled=True)
    returned = arrived[:, 0, :own_width]
    half = arrived[:, 0, own_width:]
    compressed = returned.reshape(chans, pulses, per_dev_blocks, 2, BLOCK)
    compressed = compressed.transpose(3, 0, 1, 2, 4).reshape(2, chans, pulses, cells_dev)

    partner = lax.ppermute(half, "chan", [(0, 1), (1, 0)])
    upper = lax.axis_index("chan") == 0
    every = jnp.concatenate(
        [jnp.where(upper, half, partner), jnp.where(upper, partner, half)], axis=0
    )

    snap_re = snap[:, :TRAIN]
    snap_im = snap[:, TRAIN:]
    left = jnp.concatenate([snap, jnp.concatenate([snap_im, -snap_re], axis=1)], axis=0)
    gram = lax.dot_general(
        left, every, (((1,), (1,)), ((), ())), preferred_element_type=jnp.float32
    )
    covariance = (gram * (1.0 / TRAIN)).reshape(2, 1, series_dev, -1)
    return (compressed, covariance)


def solution(mesh):
    placed = (P("groups", "chan", None, "range"), P(), P("groups", None))
    return jax.shard_map(
        on_device,
        mesh=mesh,
        in_specs=placed,
        out_specs=(P("groups", "chan", None, "range"), P("groups", "chan", "range", None)),
        check_vma=False,
    )
```

```python
from functools import partial

import jax
import jax.numpy as jnp
from jax import lax
from jax.experimental import pallas as pl
from jax.experimental.pallas import tpu as pltpu
from jax.sharding import PartitionSpec as P

TRAIN = 128
BLOCK = 128


def train_cells(gates, count):
    starts = gates[0]
    widths = gates[1]
    ends = jnp.cumsum(widths)
    places = jnp.arange(count, dtype=jnp.int32)
    which = jnp.sum((ends[None, :] <= places[:, None]).astype(jnp.int32), axis=1)
    onehot = jnp.arange(gates.shape[1], dtype=jnp.int32)[None, :] == which[:, None]
    offset = jnp.sum(jnp.where(onehot, (starts - (ends - widths))[None, :], 0), axis=1)
    return offset + places


def toeplitz_blocks(chirp, lags):
    taps = chirp.shape[1]
    length = BLOCK * lags + BLOCK - 1
    pad_after = max(0, length - (BLOCK - 1) - taps)
    u = jnp.pad(chirp, ((0, 0), (BLOCK - 1, pad_after)))[:, :length]
    tiled = jnp.tile(u, (1, BLOCK + 1))[:, : BLOCK * (length + 1)]
    windows = tiled.reshape(2, BLOCK, length + 1)[:, :, : BLOCK * lags]
    full = windows[:, ::-1, :]
    blocks = full.reshape(2, BLOCK, lags, BLOCK).transpose(0, 2, 1, 3)
    t_re = blocks[0]
    t_im = blocks[1]
    top = jnp.concatenate([t_re, t_im], axis=2)
    bottom = jnp.concatenate([-t_im, t_re], axis=2)
    w = jnp.concatenate([top, bottom], axis=1)
    hi = w.astype(jnp.bfloat16)
    lo = (w - hi.astype(jnp.float32)).astype(jnp.bfloat16)
    return jnp.concatenate([hi, lo], axis=2)


def conv_kernel(x_ref, w_ref, o_ref, *, lags):
    d = pl.program_id(0)
    start = pl.multiple_of(d * BLOCK, BLOCK)
    span = lags * BLOCK
    acc = jnp.dot(x_ref[0, :, pl.ds(start, span)], w_ref[0], preferred_element_type=jnp.float32)
    acc = acc + jnp.dot(
        x_ref[1, :, pl.ds(start, span)], w_ref[1], preferred_element_type=jnp.float32
    )
    out = acc[:, : 2 * BLOCK] + acc[:, 2 * BLOCK :]
    o_ref[0] = out[:, :BLOCK].astype(o_ref.dtype)
    o_ref[1] = out[:, BLOCK:].astype(o_ref.dtype)


def causal_filter(x, w):
    _, rows, total = x.shape
    lags = w.shape[0]
    nblocks = total // BLOCK
    flipped = w[::-1]
    stacked = jnp.stack(
        [
            flipped[:, :BLOCK].reshape(lags * BLOCK, 4 * BLOCK),
            flipped[:, BLOCK:].reshape(lags * BLOCK, 4 * BLOCK),
        ]
    )
    padded = jnp.pad(x, ((0, 0), (0, 0), ((lags - 1) * BLOCK, 0)))
    work = 2 * rows * lags * BLOCK * 4 * BLOCK * 2 * nblocks
    return pl.pallas_call(
        partial(conv_kernel, lags=lags),
        out_shape=jax.ShapeDtypeStruct((2, rows, total), jnp.bfloat16),
        grid=(nblocks,),
        in_specs=[
            pl.BlockSpec(padded.shape, lambda d: (0, 0, 0)),
            pl.BlockSpec(stacked.shape, lambda d: (0, 0, 0)),
        ],
        out_specs=pl.BlockSpec((2, rows, BLOCK), lambda d: (0, 0, d)),
        compiler_params=pltpu.CompilerParams(vmem_limit_bytes=48 * 1024 * 1024),
        cost_estimate=pl.CostEstimate(
            flops=work, transcendentals=0, bytes_accessed=2 * x.size * 2 + w.size * 2
        ),
    )(padded, stacked)


def on_device(echoes, chirp, gates):
    chans = echoes.shape[1]
    pulses = echoes.shape[2]
    cells_dev = echoes.shape[3]
    taps = chirp.shape[1]
    ranks = lax.axis_size("range")
    range_len = cells_dev * ranks
    nblocks = range_len // BLOCK
    lags = min((taps - 1 + BLOCK - 1) // BLOCK + 1, nblocks)
    series_total = chans * pulses
    series_dev = series_total // ranks

    w = toeplitz_blocks(chirp, lags)

    local = echoes.reshape(2, series_total, cells_dev)
    x = lax.all_to_all(local, "range", split_axis=1, concat_axis=2, tiled=True)
    y = causal_filter(x, w)

    cells = train_cells(gates, TRAIN)
    pick = (jnp.arange(range_len, dtype=jnp.int32)[:, None] == cells[None, :]).astype(y.dtype)
    snap = jnp.dot(
        y.reshape(2 * series_dev, range_len), pick, preferred_element_type=jnp.float32
    ).astype(y.dtype).reshape(2, series_dev, TRAIN)

    spread = jnp.broadcast_to(snap[:, :, None, :], (2, series_dev, ranks, TRAIN))
    both = jnp.concatenate([y.reshape(2, series_dev, ranks, cells_dev), spread], axis=3)
    arrived = lax.all_to_all(both, "range", split_axis=2, concat_axis=1, tiled=True)
    compressed = arrived[:, :, 0, :cells_dev].reshape(2, chans, pulses, cells_dev)
    half = arrived[:, :, 0, cells_dev:]

    partner = lax.ppermute(half, "chan", [(0, 1), (1, 0)])
    upper = lax.axis_index("chan") == 0
    every = jnp.concatenate(
        [jnp.where(upper, half, partner), jnp.where(upper, partner, half)], axis=1
    )

    left = jnp.stack([snap, jnp.stack([snap[1], -snap[0]])])
    gram = lax.dot_general(
        left, every, (((1, 3), (0, 2)), ((), ())), preferred_element_type=jnp.float32
    )
    covariance = (gram * (1.0 / TRAIN)).reshape(2, 1, series_dev, -1)
    return (compressed, covariance)


def solution(mesh):
    placed = (P("groups", "chan", None, "range"), P(), P("groups", None))
    return jax.shard_map(
        on_device,
        mesh=mesh,
        in_specs=placed,
        out_specs=(P("groups", "chan", None, "range"), P("groups", "chan", "range", None)),
        check_vma=False,
    )
```

```python
from functools import partial

import jax
import jax.numpy as jnp
from jax import lax
from jax.experimental import pallas as pl
from jax.experimental.pallas import tpu as pltpu
from jax.sharding import PartitionSpec as P

TRAIN = 128
BLOCK = 128


def train_cells(gates, count):
    starts = gates[0]
    widths = gates[1]
    ends = jnp.cumsum(widths)
    places = jnp.arange(count, dtype=jnp.int32)
    which = jnp.sum((ends[None, :] <= places[:, None]).astype(jnp.int32), axis=1)
    onehot = jnp.arange(gates.shape[1], dtype=jnp.int32)[None, :] == which[:, None]
    offset = jnp.sum(jnp.where(onehot, (starts - (ends - widths))[None, :], 0), axis=1)
    return offset + places


def toeplitz_blocks(chirp, lags):
    taps = chirp.shape[1]
    length = BLOCK * lags + BLOCK - 1
    pad_after = max(0, length - (BLOCK - 1) - taps)
    u = jnp.pad(chirp, ((0, 0), (BLOCK - 1, pad_after)))[:, :length]
    tiled = jnp.tile(u, (1, BLOCK + 1))[:, : BLOCK * (length + 1)]
    windows = tiled.reshape(2, BLOCK, length + 1)[:, :, : BLOCK * lags]
    full = windows[:, ::-1, :]
    blocks = full.reshape(2, BLOCK, lags, BLOCK).transpose(0, 2, 1, 3)
    t_re = blocks[0]
    t_im = blocks[1]
    top = jnp.concatenate([t_re, t_im], axis=2)
    bottom = jnp.concatenate([-t_im, t_re], axis=2)
    w = jnp.concatenate([top, bottom], axis=1)
    hi = w.astype(jnp.bfloat16)
    lo = (w - hi.astype(jnp.float32)).astype(jnp.bfloat16)
    return jnp.concatenate([hi, lo], axis=2)


def conv_kernel(x_ref, w_ref, o_ref, *, lags):
    d = pl.program_id(0)
    start = pl.multiple_of(d * BLOCK, BLOCK)
    span = lags * BLOCK
    acc = jnp.dot(x_ref[0, :, pl.ds(start, span)], w_ref[0], preferred_element_type=jnp.float32)
    acc = acc + jnp.dot(
        x_ref[1, :, pl.ds(start, span)], w_ref[1], preferred_element_type=jnp.float32
    )
    out = acc[:, : 2 * BLOCK] + acc[:, 2 * BLOCK :]
    o_ref[0] = out[:, :BLOCK].astype(o_ref.dtype)
    o_ref[1] = out[:, BLOCK:].astype(o_ref.dtype)


def causal_filter(x, w):
    _, rows, total = x.shape
    lags = w.shape[0]
    nblocks = total // BLOCK
    flipped = w[::-1]
    stacked = jnp.stack(
        [
            flipped[:, :BLOCK].reshape(lags * BLOCK, 4 * BLOCK),
            flipped[:, BLOCK:].reshape(lags * BLOCK, 4 * BLOCK),
        ]
    )
    padded = jnp.pad(x, ((0, 0), (0, 0), ((lags - 1) * BLOCK, 0)))
    work = 2 * rows * lags * BLOCK * 4 * BLOCK * 2 * nblocks
    return pl.pallas_call(
        partial(conv_kernel, lags=lags),
        out_shape=jax.ShapeDtypeStruct((2, rows, total), jnp.bfloat16),
        grid=(nblocks,),
        in_specs=[
            pl.BlockSpec(padded.shape, lambda d: (0, 0, 0)),
            pl.BlockSpec(stacked.shape, lambda d: (0, 0, 0)),
        ],
        out_specs=pl.BlockSpec((2, rows, BLOCK), lambda d: (0, 0, d)),
        compiler_params=pltpu.CompilerParams(vmem_limit_bytes=48 * 1024 * 1024),
        cost_estimate=pl.CostEstimate(
            flops=work, transcendentals=0, bytes_accessed=2 * x.size * 2 + w.size * 2
        ),
    )(padded, stacked)


def on_device(echoes, chirp, gates):
    chans = echoes.shape[1]
    pulses = echoes.shape[2]
    cells_dev = echoes.shape[3]
    taps = chirp.shape[1]
    ranks = lax.axis_size("range")
    range_len = cells_dev * ranks
    nblocks = range_len // BLOCK
    lags = min((taps - 1 + BLOCK - 1) // BLOCK + 1, nblocks)
    series_total = chans * pulses
    series_dev = series_total // ranks

    w = toeplitz_blocks(chirp, lags)

    local = echoes.reshape(2, series_total, cells_dev)
    x = lax.all_to_all(local, "range", split_axis=1, concat_axis=2, tiled=True)
    y = causal_filter(x, w)

    cells = train_cells(gates, TRAIN)
    pick = (jnp.arange(range_len, dtype=jnp.int32)[:, None] == cells[None, :]).astype(y.dtype)
    snap = jnp.dot(
        y.reshape(2 * series_dev, range_len), pick, preferred_element_type=jnp.float32
    ).astype(y.dtype).reshape(2, series_dev, TRAIN)

    spread = jnp.broadcast_to(snap[:, :, None, :], (2, series_dev, ranks, TRAIN))
    half = lax.all_to_all(spread, "range", split_axis=2, concat_axis=1, tiled=True)[:, :, 0]
    home = lax.all_to_all(
        y.reshape(2, series_dev, ranks, cells_dev), "range", split_axis=2, concat_axis=1, tiled=True
    )
    compressed = home.reshape(2, chans, pulses, cells_dev)

    partner = lax.ppermute(half, "chan", [(0, 1), (1, 0)])
    upper = lax.axis_index("chan") == 0
    every = jnp.concatenate(
        [jnp.where(upper, half, partner), jnp.where(upper, partner, half)], axis=1
    )

    left = jnp.stack([snap, jnp.stack([snap[1], -snap[0]])])
    gram = lax.dot_general(
        left, every, (((1, 3), (0, 2)), ((), ())), preferred_element_type=jnp.float32
    )
    covariance = (gram * (1.0 / TRAIN)).reshape(2, 1, series_dev, -1)
    return (compressed, covariance)


def solution(mesh):
    placed = (P("groups", "chan", None, "range"), P(), P("groups", None))
    return jax.shard_map(
        on_device,
        mesh=mesh,
        in_specs=placed,
        out_specs=(P("groups", "chan", None, "range"), P("groups", "chan", "range", None)),
        check_vma=False,
    )
```

```python
from functools import partial

import jax
import jax.numpy as jnp
from jax import lax
from jax.experimental import pallas as pl
from jax.experimental.pallas import tpu as pltpu
from jax.sharding import PartitionSpec as P

TRAIN = 128
BLOCK = 128


def train_cells(gates, count):
    starts = gates[0]
    widths = gates[1]
    ends = jnp.cumsum(widths)
    places = jnp.arange(count, dtype=jnp.int32)
    which = jnp.sum((ends[None, :] <= places[:, None]).astype(jnp.int32), axis=1)
    onehot = jnp.arange(gates.shape[1], dtype=jnp.int32)[None, :] == which[:, None]
    offset = jnp.sum(jnp.where(onehot, (starts - (ends - widths))[None, :], 0), axis=1)
    return offset + places


def toeplitz_blocks(chirp, lags):
    taps = chirp.shape[1]
    length = BLOCK * lags + BLOCK - 1
    pad_after = max(0, length - (BLOCK - 1) - taps)
    u = jnp.pad(chirp, ((0, 0), (BLOCK - 1, pad_after)))[:, :length]
    tiled = jnp.tile(u, (1, BLOCK + 1))[:, : BLOCK * (length + 1)]
    windows = tiled.reshape(2, BLOCK, length + 1)[:, :, : BLOCK * lags]
    full = windows[:, ::-1, :]
    blocks = full.reshape(2, BLOCK, lags, BLOCK).transpose(0, 2, 1, 3)
    t_re = blocks[0]
    t_im = blocks[1]
    top = jnp.concatenate([t_re, t_im], axis=2)
    bottom = jnp.concatenate([-t_im, t_re], axis=2)
    w = jnp.concatenate([top, bottom], axis=1)
    hi = w.astype(jnp.bfloat16)
    lo = (w - hi.astype(jnp.float32)).astype(jnp.bfloat16)
    return jnp.concatenate([hi, lo], axis=2)


def conv_kernel(x_ref, w_ref, o_ref, *, lags):
    d = pl.program_id(0)
    start = pl.multiple_of(d * BLOCK, BLOCK)
    span = lags * BLOCK
    acc = jnp.dot(x_ref[0, :, pl.ds(start, span)], w_ref[0], preferred_element_type=jnp.float32)
    acc = acc + jnp.dot(
        x_ref[1, :, pl.ds(start, span)], w_ref[1], preferred_element_type=jnp.float32
    )
    out = acc[:, : 2 * BLOCK] + acc[:, 2 * BLOCK :]
    o_ref[0] = out[:, :BLOCK].astype(o_ref.dtype)
    o_ref[1] = out[:, BLOCK:].astype(o_ref.dtype)


def causal_filter(x, w):
    _, rows, total = x.shape
    lags = w.shape[0]
    nblocks = total // BLOCK
    flipped = w[::-1]
    stacked = jnp.stack(
        [
            flipped[:, :BLOCK].reshape(lags * BLOCK, 4 * BLOCK),
            flipped[:, BLOCK:].reshape(lags * BLOCK, 4 * BLOCK),
        ]
    )
    padded = jnp.pad(x, ((0, 0), (0, 0), ((lags - 1) * BLOCK, 0)))
    work = 2 * rows * lags * BLOCK * 4 * BLOCK * 2 * nblocks
    return pl.pallas_call(
        partial(conv_kernel, lags=lags),
        out_shape=jax.ShapeDtypeStruct((2, rows, total), jnp.bfloat16),
        grid=(nblocks,),
        in_specs=[
            pl.BlockSpec(padded.shape, lambda d: (0, 0, 0)),
            pl.BlockSpec(stacked.shape, lambda d: (0, 0, 0)),
        ],
        out_specs=pl.BlockSpec((2, rows, BLOCK), lambda d: (0, 0, d)),
        compiler_params=pltpu.CompilerParams(vmem_limit_bytes=48 * 1024 * 1024),
        cost_estimate=pl.CostEstimate(
            flops=work, transcendentals=0, bytes_accessed=2 * x.size * 2 + w.size * 2
        ),
    )(padded, stacked)


def gram_kernel(first_ref, left_ref, cols_ref, *rest):
    out_ref = rest[-1]
    for o in range(2):
        acc = None
        for k in range(2):
            part = lax.dot_general(
                left_ref[o, k],
                cols_ref[k],
                (((1,), (1,)), ((), ())),
                preferred_element_type=jnp.float32,
            )
            acc = part if acc is None else acc + part
        out_ref[o, 0] = acc * (1.0 / TRAIN)


def gram_half(left, cols, first, total_cols, into=None):
    rows = left.shape[2]
    ncols = cols.shape[1]
    tile = min(512, ncols)
    steps = ncols // tile
    operands = [left, cols]
    in_specs = [
        pl.BlockSpec(left.shape, lambda i, f: (0, 0, 0, 0)),
        pl.BlockSpec((2, tile, TRAIN), lambda i, f: (0, i, 0)),
    ]
    aliases = {}
    if into is not None:
        operands.append(into)
        in_specs.append(pl.BlockSpec(memory_space=pl.ANY))
        aliases = {3: 0}
    return pl.pallas_call(
        gram_kernel,
        out_shape=jax.ShapeDtypeStruct((2, 1, rows, total_cols), jnp.float32),
        grid_spec=pltpu.PrefetchScalarGridSpec(
            num_scalar_prefetch=1,
            grid=(steps,),
            in_specs=in_specs,
            out_specs=pl.BlockSpec((2, 1, rows, tile), lambda i, f: (0, 0, 0, f[0] * steps + i)),
        ),
        input_output_aliases=aliases,
        cost_estimate=pl.CostEstimate(
            flops=2 * 2 * 2 * rows * ncols * TRAIN * 2,
            transcendentals=0,
            bytes_accessed=2 * rows * ncols * 4 + cols.size * 2,
        ),
    )(first, *operands)


def on_device(echoes, chirp, gates):
    chans = echoes.shape[1]
    pulses = echoes.shape[2]
    cells_dev = echoes.shape[3]
    taps = chirp.shape[1]
    ranks = lax.axis_size("range")
    range_len = cells_dev * ranks
    nblocks = range_len // BLOCK
    lags = min((taps - 1 + BLOCK - 1) // BLOCK + 1, nblocks)
    series_total = chans * pulses
    series_dev = series_total // ranks

    w = toeplitz_blocks(chirp, lags)

    local = echoes.reshape(2, series_total, cells_dev)
    x = lax.all_to_all(local, "range", split_axis=1, concat_axis=2, tiled=True)
    y = causal_filter(x, w)

    cells = train_cells(gates, TRAIN)
    pick = (jnp.arange(range_len, dtype=jnp.int32)[:, None] == cells[None, :]).astype(y.dtype)
    snap = jnp.dot(
        y.reshape(2 * series_dev, range_len), pick, preferred_element_type=jnp.float32
    ).astype(y.dtype).reshape(2, series_dev, TRAIN)

    spread = jnp.broadcast_to(snap[:, :, None, :], (2, series_dev, ranks, TRAIN))
    both = jnp.concatenate([y.reshape(2, series_dev, ranks, cells_dev), spread], axis=3)
    arrived = lax.all_to_all(both, "range", split_axis=2, concat_axis=1, tiled=True)
    compressed = arrived[:, :, 0, :cells_dev].reshape(2, chans, pulses, cells_dev)
    half = arrived[:, :, 0, cells_dev:]

    partner = lax.ppermute(half, "chan", [(0, 1), (1, 0)])
    q = lax.axis_index("chan").astype(jnp.int32)
    left = jnp.stack([snap, jnp.stack([snap[1], -snap[0]])])
    total_cols = 2 * half.shape[1]
    own = gram_half(left, half, q.reshape(1), total_cols)
    covariance = gram_half(left, partner, (1 - q).reshape(1), total_cols, into=own)
    return (compressed, covariance)


def solution(mesh):
    placed = (P("groups", "chan", None, "range"), P(), P("groups", None))
    return jax.shard_map(
        on_device,
        mesh=mesh,
        in_specs=placed,
        out_specs=(P("groups", "chan", None, "range"), P("groups", "chan", "range", None)),
        check_vma=False,
    )
```

```python
from functools import partial

import jax
import jax.numpy as jnp
from jax import lax
from jax.experimental import pallas as pl
from jax.experimental.pallas import tpu as pltpu
from jax.sharding import PartitionSpec as P

TRAIN = 128
BLOCK = 128


def train_cells(gates, count):
    starts = gates[0]
    widths = gates[1]
    ends = jnp.cumsum(widths)
    places = jnp.arange(count, dtype=jnp.int32)
    which = jnp.sum((ends[None, :] <= places[:, None]).astype(jnp.int32), axis=1)
    onehot = jnp.arange(gates.shape[1], dtype=jnp.int32)[None, :] == which[:, None]
    offset = jnp.sum(jnp.where(onehot, (starts - (ends - widths))[None, :], 0), axis=1)
    return offset + places


def toeplitz_blocks(chirp, lags):
    taps = chirp.shape[1]
    length = BLOCK * lags + BLOCK - 1
    pad_after = max(0, length - (BLOCK - 1) - taps)
    u = jnp.pad(chirp, ((0, 0), (BLOCK - 1, pad_after)))[:, :length]
    tiled = jnp.tile(u, (1, BLOCK + 1))[:, : BLOCK * (length + 1)]
    windows = tiled.reshape(2, BLOCK, length + 1)[:, :, : BLOCK * lags]
    full = windows[:, ::-1, :]
    blocks = full.reshape(2, BLOCK, lags, BLOCK).transpose(0, 2, 1, 3)
    t_re = blocks[0]
    t_im = blocks[1]
    top = jnp.concatenate([t_re, t_im], axis=2)
    bottom = jnp.concatenate([-t_im, t_re], axis=2)
    w = jnp.concatenate([top, bottom], axis=1)
    hi = w.astype(jnp.bfloat16)
    lo = (w - hi.astype(jnp.float32)).astype(jnp.bfloat16)
    return jnp.concatenate([hi, lo], axis=2)


def conv_kernel(x_ref, w_ref, o_ref, *, lags):
    d = pl.program_id(0)
    start = pl.multiple_of(d * BLOCK, BLOCK)
    head = lags // 2

    def window(lo, hi):
        part = None
        for k in range(2):
            xs = x_ref[k, :, pl.ds(start + lo * BLOCK, (hi - lo) * BLOCK)]
            term = jnp.dot(xs, w_ref[k, lo * BLOCK : hi * BLOCK], preferred_element_type=jnp.float32)
            part = term if part is None else part + term
        return part

    acc = window(head, lags)
    if head > 0:
        acc = lax.cond(d >= lags - head, lambda a: a + window(0, head), lambda a: a, acc)
    out = acc[:, : 2 * BLOCK] + acc[:, 2 * BLOCK :]
    o_ref[0] = out[:, :BLOCK].astype(o_ref.dtype)
    o_ref[1] = out[:, BLOCK:].astype(o_ref.dtype)


def causal_filter(x, w):
    _, rows, total = x.shape
    lags = w.shape[0]
    nblocks = total // BLOCK
    flipped = w[::-1]
    stacked = jnp.stack(
        [
            flipped[:, :BLOCK].reshape(lags * BLOCK, 4 * BLOCK),
            flipped[:, BLOCK:].reshape(lags * BLOCK, 4 * BLOCK),
        ]
    )
    padded = jnp.pad(x, ((0, 0), (0, 0), ((lags - 1) * BLOCK, 0)))
    work = 2 * rows * lags * BLOCK * 4 * BLOCK * 2 * nblocks
    return pl.pallas_call(
        partial(conv_kernel, lags=lags),
        out_shape=jax.ShapeDtypeStruct((2, rows, total), jnp.bfloat16),
        grid=(nblocks,),
        in_specs=[
            pl.BlockSpec(padded.shape, lambda d: (0, 0, 0)),
            pl.BlockSpec(stacked.shape, lambda d: (0, 0, 0)),
        ],
        out_specs=pl.BlockSpec((2, rows, BLOCK), lambda d: (0, 0, d)),
        compiler_params=pltpu.CompilerParams(vmem_limit_bytes=48 * 1024 * 1024),
        cost_estimate=pl.CostEstimate(
            flops=work, transcendentals=0, bytes_accessed=2 * x.size * 2 + w.size * 2
        ),
    )(padded, stacked)


def on_device(echoes, chirp, gates):
    chans = echoes.shape[1]
    pulses = echoes.shape[2]
    cells_dev = echoes.shape[3]
    taps = chirp.shape[1]
    ranks = lax.axis_size("range")
    range_len = cells_dev * ranks
    nblocks = range_len // BLOCK
    lags = min((taps - 1 + BLOCK - 1) // BLOCK + 1, nblocks)
    series_total = chans * pulses
    series_dev = series_total // ranks

    w = toeplitz_blocks(chirp, lags)

    local = echoes.reshape(2, series_total, cells_dev)
    x = lax.all_to_all(local, "range", split_axis=1, concat_axis=2, tiled=True)
    y = causal_filter(x, w)

    cells = train_cells(gates, TRAIN)
    pick = (jnp.arange(range_len, dtype=jnp.int32)[:, None] == cells[None, :]).astype(y.dtype)
    snap = jnp.dot(
        y.reshape(2 * series_dev, range_len), pick, preferred_element_type=jnp.float32
    ).astype(y.dtype).reshape(2, series_dev, TRAIN)

    spread = jnp.broadcast_to(snap[:, :, None, :], (2, series_dev, ranks, TRAIN))
    both = jnp.concatenate([y.reshape(2, series_dev, ranks, cells_dev), spread], axis=3)
    arrived = lax.all_to_all(both, "range", split_axis=2, concat_axis=1, tiled=True)
    compressed = arrived[:, :, 0, :cells_dev].reshape(2, chans, pulses, cells_dev)
    half = arrived[:, :, 0, cells_dev:]

    partner = lax.ppermute(half, "chan", [(0, 1), (1, 0)])
    upper = lax.axis_index("chan") == 0
    every = jnp.concatenate(
        [jnp.where(upper, half, partner), jnp.where(upper, partner, half)], axis=1
    )

    left = jnp.stack([snap, jnp.stack([snap[1], -snap[0]])])
    gram = lax.dot_general(
        left, every, (((1, 3), (0, 2)), ((), ())), preferred_element_type=jnp.float32
    )
    covariance = (gram * (1.0 / TRAIN)).reshape(2, 1, series_dev, -1)
    return (compressed, covariance)


def solution(mesh):
    placed = (P("groups", "chan", None, "range"), P(), P("groups", None))
    return jax.shard_map(
        on_device,
        mesh=mesh,
        in_specs=placed,
        out_specs=(P("groups", "chan", None, "range"), P("groups", "chan", "range", None)),
        check_vma=False,
    )
```

```python
from functools import partial

import jax
import jax.numpy as jnp
from jax import lax
from jax.experimental import pallas as pl
from jax.experimental.pallas import tpu as pltpu
from jax.sharding import PartitionSpec as P

TRAIN = 128
BLOCK = 128


def train_cells(gates, count):
    starts = gates[0]
    widths = gates[1]
    ends = jnp.cumsum(widths)
    places = jnp.arange(count, dtype=jnp.int32)
    which = jnp.sum((ends[None, :] <= places[:, None]).astype(jnp.int32), axis=1)
    onehot = jnp.arange(gates.shape[1], dtype=jnp.int32)[None, :] == which[:, None]
    offset = jnp.sum(jnp.where(onehot, (starts - (ends - widths))[None, :], 0), axis=1)
    return offset + places


def toeplitz_blocks(chirp, lags):
    taps = chirp.shape[1]
    length = BLOCK * lags + BLOCK - 1
    pad_after = max(0, length - (BLOCK - 1) - taps)
    u = jnp.pad(chirp, ((0, 0), (BLOCK - 1, pad_after)))[:, :length]
    tiled = jnp.tile(u, (1, BLOCK + 1))[:, : BLOCK * (length + 1)]
    windows = tiled.reshape(2, BLOCK, length + 1)[:, :, : BLOCK * lags]
    full = windows[:, ::-1, :]
    blocks = full.reshape(2, BLOCK, lags, BLOCK).transpose(0, 2, 1, 3)
    t_re = blocks[0]
    t_im = blocks[1]
    top = jnp.concatenate([t_re, t_im], axis=2)
    bottom = jnp.concatenate([-t_im, t_re], axis=2)
    w = jnp.concatenate([top, bottom], axis=1)
    hi = lax.reduce_precision(w, exponent_bits=8, mantissa_bits=7)
    lo = (w - hi).astype(jnp.bfloat16)
    return jnp.concatenate([hi.astype(jnp.bfloat16), lo], axis=2)


def conv_kernel(x_ref, w_ref, o_ref, *, lags):
    d = pl.program_id(0)
    start = pl.multiple_of(d * BLOCK, BLOCK)
    span = lags * BLOCK
    acc = jnp.dot(x_ref[0, :, pl.ds(start, span)], w_ref[0], preferred_element_type=jnp.float32)
    acc = acc + jnp.dot(
        x_ref[1, :, pl.ds(start, span)], w_ref[1], preferred_element_type=jnp.float32
    )
    out = acc[:, : 2 * BLOCK] + acc[:, 2 * BLOCK :]
    o_ref[0] = out[:, :BLOCK].astype(o_ref.dtype)
    o_ref[1] = out[:, BLOCK:].astype(o_ref.dtype)


def causal_filter(x, w):
    _, rows, total = x.shape
    lags = w.shape[0]
    nblocks = total // BLOCK
    flipped = w[::-1]
    stacked = jnp.stack(
        [
            flipped[:, :BLOCK].reshape(lags * BLOCK, 4 * BLOCK),
            flipped[:, BLOCK:].reshape(lags * BLOCK, 4 * BLOCK),
        ]
    )
    padded = jnp.pad(x, ((0, 0), (0, 0), ((lags - 1) * BLOCK, 0)))
    work = 2 * rows * lags * BLOCK * 4 * BLOCK * 2 * nblocks
    return pl.pallas_call(
        partial(conv_kernel, lags=lags),
        out_shape=jax.ShapeDtypeStruct((2, rows, total), jnp.bfloat16),
        grid=(nblocks,),
        in_specs=[
            pl.BlockSpec(padded.shape, lambda d: (0, 0, 0)),
            pl.BlockSpec(stacked.shape, lambda d: (0, 0, 0)),
        ],
        out_specs=pl.BlockSpec((2, rows, BLOCK), lambda d: (0, 0, d)),
        compiler_params=pltpu.CompilerParams(vmem_limit_bytes=48 * 1024 * 1024),
        cost_estimate=pl.CostEstimate(
            flops=work, transcendentals=0, bytes_accessed=2 * x.size * 2 + w.size * 2
        ),
    )(padded, stacked)


def on_device(echoes, chirp, gates):
    chans = echoes.shape[1]
    pulses = echoes.shape[2]
    cells_dev = echoes.shape[3]
    taps = chirp.shape[1]
    ranks = lax.axis_size("range")
    range_len = cells_dev * ranks
    nblocks = range_len // BLOCK
    lags = min((taps - 1 + BLOCK - 1) // BLOCK + 1, nblocks)
    series_total = chans * pulses
    series_dev = series_total // ranks

    w = toeplitz_blocks(chirp, lags)

    local = echoes.reshape(2, series_total, cells_dev)
    x = lax.all_to_all(local, "range", split_axis=1, concat_axis=2, tiled=True)
    y = causal_filter(x, w)

    cells = train_cells(gates, TRAIN)
    pick = (jnp.arange(range_len, dtype=jnp.int32)[:, None] == cells[None, :]).astype(y.dtype)
    snap = jnp.dot(
        y.reshape(2 * series_dev, range_len), pick, preferred_element_type=jnp.float32
    ).astype(y.dtype).reshape(2, series_dev, TRAIN)

    spread = jnp.broadcast_to(snap[:, :, None, :], (2, series_dev, ranks, TRAIN))
    both = jnp.concatenate([y.reshape(2, series_dev, ranks, cells_dev), spread], axis=3)
    arrived = lax.all_to_all(both, "range", split_axis=2, concat_axis=1, tiled=True)
    compressed = arrived[:, :, 0, :cells_dev].reshape(2, chans, pulses, cells_dev)
    half = arrived[:, :, 0, cells_dev:]

    partner = lax.ppermute(half, "chan", [(0, 1), (1, 0)])
    upper = lax.axis_index("chan") == 0
    every = jnp.concatenate(
        [jnp.where(upper, half, partner), jnp.where(upper, partner, half)], axis=1
    )

    left = jnp.stack([snap, jnp.stack([snap[1], -snap[0]])])
    gram = lax.dot_general(
        left, every, (((1, 3), (0, 2)), ((), ())), preferred_element_type=jnp.float32
    )
    covariance = (gram * (1.0 / TRAIN)).reshape(2, 1, series_dev, -1)
    return (compressed, covariance)


def solution(mesh):
    placed = (P("groups", "chan", None, "range"), P(), P("groups", None))
    return jax.shard_map(
        on_device,
        mesh=mesh,
        in_specs=placed,
        out_specs=(P("groups", "chan", None, "range"), P("groups", "chan", "range", None)),
        check_vma=False,
    )
```

```python
from functools import partial

import jax
import jax.numpy as jnp
from jax import lax
from jax.experimental import pallas as pl
from jax.experimental.pallas import tpu as pltpu
from jax.sharding import PartitionSpec as P

TRAIN = 128
BLOCK = 128


def train_cells(gates, count):
    starts = gates[0]
    widths = gates[1]
    ends = jnp.cumsum(widths)
    places = jnp.arange(count, dtype=jnp.int32)
    which = jnp.sum((ends[None, :] <= places[:, None]).astype(jnp.int32), axis=1)
    onehot = jnp.arange(gates.shape[1], dtype=jnp.int32)[None, :] == which[:, None]
    offset = jnp.sum(jnp.where(onehot, (starts - (ends - widths))[None, :], 0), axis=1)
    return offset + places


def toeplitz_blocks(chirp, lags):
    taps = chirp.shape[1]
    length = BLOCK * lags + BLOCK - 1
    pad_after = max(0, length - (BLOCK - 1) - taps)
    u = jnp.pad(chirp, ((0, 0), (BLOCK - 1, pad_after)))[:, :length]
    tiled = jnp.tile(u, (1, BLOCK + 1))[:, : BLOCK * (length + 1)]
    windows = tiled.reshape(2, BLOCK, length + 1)[:, :, : BLOCK * lags]
    full = windows[:, ::-1, :]
    blocks = full.reshape(2, BLOCK, lags, BLOCK).transpose(0, 2, 1, 3)
    t_re = blocks[0]
    t_im = blocks[1]
    top = jnp.concatenate([t_re, t_im], axis=2)
    bottom = jnp.concatenate([-t_im, t_re], axis=2)
    w = jnp.concatenate([top, bottom], axis=1)
    hi = lax.reduce_precision(w, exponent_bits=8, mantissa_bits=7)
    lo = (w - hi).astype(jnp.bfloat16)
    return jnp.concatenate([hi.astype(jnp.bfloat16), lo], axis=2)


def conv_kernel(x_ref, w_ref, o_ref, *, lags):
    d = pl.program_id(0)
    start = pl.multiple_of(d * BLOCK, BLOCK)
    span = lags * BLOCK
    acc = jnp.dot(x_ref[0, :, pl.ds(start, span)], w_ref[0], preferred_element_type=jnp.float32)
    acc = acc + jnp.dot(
        x_ref[1, :, pl.ds(start, span)], w_ref[1], preferred_element_type=jnp.float32
    )
    out = acc[:, : 2 * BLOCK] + acc[:, 2 * BLOCK :]
    o_ref[0] = out[:, :BLOCK].astype(o_ref.dtype)
    o_ref[1] = out[:, BLOCK:].astype(o_ref.dtype)


def causal_filter(x, w):
    _, rows, total = x.shape
    lags = w.shape[0]
    nblocks = total // BLOCK
    flipped = w[::-1]
    stacked = jnp.stack(
        [
            flipped[:, :BLOCK].reshape(lags * BLOCK, 4 * BLOCK),
            flipped[:, BLOCK:].reshape(lags * BLOCK, 4 * BLOCK),
        ]
    )
    padded = jnp.pad(x, ((0, 0), (0, 0), ((lags - 1) * BLOCK, 0)))
    work = 2 * rows * lags * BLOCK * 4 * BLOCK * 2 * nblocks
    return pl.pallas_call(
        partial(conv_kernel, lags=lags),
        out_shape=jax.ShapeDtypeStruct((2, rows, total), jnp.bfloat16),
        grid=(nblocks,),
        in_specs=[
            pl.BlockSpec(padded.shape, lambda d: (0, 0, 0)),
            pl.BlockSpec(stacked.shape, lambda d: (0, 0, 0)),
        ],
        out_specs=pl.BlockSpec((2, rows, BLOCK), lambda d: (0, 0, d)),
        compiler_params=pltpu.CompilerParams(vmem_limit_bytes=48 * 1024 * 1024),
        cost_estimate=pl.CostEstimate(
            flops=work, transcendentals=0, bytes_accessed=2 * x.size * 2 + w.size * 2
        ),
    )(padded, stacked)


def on_device(echoes, chirp, gates):
    chans = echoes.shape[1]
    pulses = echoes.shape[2]
    cells_dev = echoes.shape[3]
    taps = chirp.shape[1]
    ranks = lax.axis_size("range")
    range_len = cells_dev * ranks
    nblocks = range_len // BLOCK
    lags = min((taps - 1 + BLOCK - 1) // BLOCK + 1, nblocks)
    series_total = chans * pulses
    series_dev = series_total // ranks

    w = toeplitz_blocks(chirp, lags)

    local = echoes.reshape(2, series_total, cells_dev)
    x = jnp.stack(
        [lax.all_to_all(local[k], "range", split_axis=0, concat_axis=1, tiled=True) for k in range(2)]
    )
    y = causal_filter(x, w)

    cells = train_cells(gates, TRAIN)
    pick = (jnp.arange(range_len, dtype=jnp.int32)[:, None] == cells[None, :]).astype(y.dtype)
    snap = jnp.dot(
        y.reshape(2 * series_dev, range_len), pick, preferred_element_type=jnp.float32
    ).astype(y.dtype).reshape(2, series_dev, TRAIN)

    spread = jnp.broadcast_to(snap[:, :, None, :], (2, series_dev, ranks, TRAIN))
    both = jnp.concatenate([y.reshape(2, series_dev, ranks, cells_dev), spread], axis=3)
    arrived = lax.all_to_all(both, "range", split_axis=2, concat_axis=1, tiled=True)
    compressed = arrived[:, :, 0, :cells_dev].reshape(2, chans, pulses, cells_dev)
    half = arrived[:, :, 0, cells_dev:]

    partner = lax.ppermute(half, "chan", [(0, 1), (1, 0)])
    upper = lax.axis_index("chan") == 0
    every = jnp.concatenate(
        [jnp.where(upper, half, partner), jnp.where(upper, partner, half)], axis=1
    )

    left = jnp.stack([snap, jnp.stack([snap[1], -snap[0]])])
    gram = lax.dot_general(
        left, every, (((1, 3), (0, 2)), ((), ())), preferred_element_type=jnp.float32
    )
    covariance = (gram * (1.0 / TRAIN)).reshape(2, 1, series_dev, -1)
    return (compressed, covariance)


def solution(mesh):
    placed = (P("groups", "chan", None, "range"), P(), P("groups", None))
    return jax.shard_map(
        on_device,
        mesh=mesh,
        in_specs=placed,
        out_specs=(P("groups", "chan", None, "range"), P("groups", "chan", "range", None)),
        check_vma=False,
    )
```

```python
from functools import partial

import jax
import jax.numpy as jnp
from jax import lax
from jax.experimental import pallas as pl
from jax.experimental.pallas import tpu as pltpu
from jax.sharding import PartitionSpec as P

TRAIN = 128
BLOCK = 128


def train_cells(gates, count):
    starts = gates[0]
    widths = gates[1]
    ends = jnp.cumsum(widths)
    places = jnp.arange(count, dtype=jnp.int32)
    which = jnp.sum((ends[None, :] <= places[:, None]).astype(jnp.int32), axis=1)
    onehot = jnp.arange(gates.shape[1], dtype=jnp.int32)[None, :] == which[:, None]
    offset = jnp.sum(jnp.where(onehot, (starts - (ends - widths))[None, :], 0), axis=1)
    return offset + places


def toeplitz_blocks(chirp, lags):
    taps = chirp.shape[1]
    length = BLOCK * lags + BLOCK - 1
    pad_after = max(0, length - (BLOCK - 1) - taps)
    u = jnp.pad(chirp, ((0, 0), (BLOCK - 1, pad_after)))[:, :length]
    tiled = jnp.tile(u, (1, BLOCK + 1))[:, : BLOCK * (length + 1)]
    windows = tiled.reshape(2, BLOCK, length + 1)[:, :, : BLOCK * lags]
    full = windows[:, ::-1, :]
    blocks = full.reshape(2, BLOCK, lags, BLOCK).transpose(0, 2, 1, 3)
    t_re = blocks[0]
    t_im = blocks[1]
    top = jnp.concatenate([t_re, t_im], axis=2)
    bottom = jnp.concatenate([-t_im, t_re], axis=2)
    w = jnp.concatenate([top, bottom], axis=1)
    hi = lax.reduce_precision(w, exponent_bits=8, mantissa_bits=7)
    lo = (w - hi).astype(jnp.bfloat16)
    return jnp.concatenate([hi.astype(jnp.bfloat16), lo], axis=2)


def conv_kernel(x_ref, w_ref, o_ref, *, lags):
    nblocks = x_ref.shape[2] // BLOCK
    span = lags * BLOCK

    def emit(d, x_start, count):
        acc = None
        for k in range(2):
            xs = x_ref[k, :, pl.ds(x_start, count * BLOCK)]
            ws = w_ref[k, span - count * BLOCK : span]
            term = jnp.dot(xs, ws, preferred_element_type=jnp.float32)
            acc = term if acc is None else acc + term
        out = acc[:, : 2 * BLOCK] + acc[:, 2 * BLOCK :]
        cols = pl.ds(pl.multiple_of(d * BLOCK, BLOCK), BLOCK)
        o_ref[0, :, cols] = out[:, :BLOCK].astype(o_ref.dtype)
        o_ref[1, :, cols] = out[:, BLOCK:].astype(o_ref.dtype)

    for d in range(min(lags - 1, nblocks)):
        emit(d, 0, d + 1)

    @pl.loop(lags - 1, nblocks)
    def _(d):
        emit(d, pl.multiple_of((d - (lags - 1)) * BLOCK, BLOCK), lags)


def causal_filter(x, w):
    _, rows, total = x.shape
    lags = w.shape[0]
    nblocks = total // BLOCK
    flipped = w[::-1]
    stacked = jnp.stack(
        [
            flipped[:, :BLOCK].reshape(lags * BLOCK, 4 * BLOCK),
            flipped[:, BLOCK:].reshape(lags * BLOCK, 4 * BLOCK),
        ]
    )
    used = sum(min(d + 1, lags) for d in range(nblocks))
    work = 2 * rows * BLOCK * 4 * BLOCK * 2 * used
    return pl.pallas_call(
        partial(conv_kernel, lags=lags),
        out_shape=jax.ShapeDtypeStruct((2, rows, total), jnp.bfloat16),
        in_specs=[
            pl.BlockSpec(memory_space=pltpu.VMEM),
            pl.BlockSpec(memory_space=pltpu.VMEM),
        ],
        out_specs=pl.BlockSpec(memory_space=pltpu.VMEM),
        compiler_params=pltpu.CompilerParams(vmem_limit_bytes=48 * 1024 * 1024),
        cost_estimate=pl.CostEstimate(
            flops=work, transcendentals=0, bytes_accessed=2 * x.size * 2 + w.size * 2
        ),
    )(x, stacked)


def on_device(echoes, chirp, gates):
    chans = echoes.shape[1]
    pulses = echoes.shape[2]
    cells_dev = echoes.shape[3]
    taps = chirp.shape[1]
    ranks = lax.axis_size("range")
    range_len = cells_dev * ranks
    nblocks = range_len // BLOCK
    lags = min((taps - 1 + BLOCK - 1) // BLOCK + 1, nblocks)
    series_total = chans * pulses
    series_dev = series_total // ranks

    w = toeplitz_blocks(chirp, lags)

    local = echoes.reshape(2, series_total, cells_dev)
    x = lax.all_to_all(local, "range", split_axis=1, concat_axis=2, tiled=True)
    y = causal_filter(x, w)

    cells = train_cells(gates, TRAIN)
    pick = (jnp.arange(range_len, dtype=jnp.int32)[:, None] == cells[None, :]).astype(y.dtype)
    snap = jnp.dot(
        y.reshape(2 * series_dev, range_len), pick, preferred_element_type=jnp.float32
    ).astype(y.dtype).reshape(2, series_dev, TRAIN)

    spread = jnp.broadcast_to(snap[:, :, None, :], (2, series_dev, ranks, TRAIN))
    both = jnp.concatenate([y.reshape(2, series_dev, ranks, cells_dev), spread], axis=3)
    arrived = lax.all_to_all(both, "range", split_axis=2, concat_axis=1, tiled=True)
    compressed = arrived[:, :, 0, :cells_dev].reshape(2, chans, pulses, cells_dev)
    half = arrived[:, :, 0, cells_dev:]

    partner = lax.ppermute(half, "chan", [(0, 1), (1, 0)])
    upper = lax.axis_index("chan") == 0
    every = jnp.concatenate(
        [jnp.where(upper, half, partner), jnp.where(upper, partner, half)], axis=1
    )

    left = jnp.stack([snap, jnp.stack([snap[1], -snap[0]])])
    gram = lax.dot_general(
        left, every, (((1, 3), (0, 2)), ((), ())), preferred_element_type=jnp.float32
    )
    covariance = (gram * (1.0 / TRAIN)).reshape(2, 1, series_dev, -1)
    return (compressed, covariance)


def solution(mesh):
    placed = (P("groups", "chan", None, "range"), P(), P("groups", None))
    return jax.shard_map(
        on_device,
        mesh=mesh,
        in_specs=placed,
        out_specs=(P("groups", "chan", None, "range"), P("groups", "chan", "range", None)),
        check_vma=False,
    )
```

```python
from functools import partial

import jax
import jax.numpy as jnp
from jax import lax
from jax.experimental import pallas as pl
from jax.experimental.pallas import tpu as pltpu
from jax.sharding import PartitionSpec as P

TRAIN = 128
BLOCK = 128


def train_cells(gates, count):
    starts = gates[0]
    widths = gates[1]
    ends = jnp.cumsum(widths)
    places = jnp.arange(count, dtype=jnp.int32)
    which = jnp.sum((ends[None, :] <= places[:, None]).astype(jnp.int32), axis=1)
    onehot = jnp.arange(gates.shape[1], dtype=jnp.int32)[None, :] == which[:, None]
    offset = jnp.sum(jnp.where(onehot, (starts - (ends - widths))[None, :], 0), axis=1)
    return offset + places


def toeplitz_blocks(chirp, lags):
    taps = chirp.shape[1]
    length = BLOCK * lags + BLOCK - 1
    pad_after = max(0, length - (BLOCK - 1) - taps)
    u = jnp.pad(chirp, ((0, 0), (BLOCK - 1, pad_after)))[:, :length]
    tiled = jnp.tile(u, (1, BLOCK + 1))[:, : BLOCK * (length + 1)]
    windows = tiled.reshape(2, BLOCK, length + 1)[:, :, : BLOCK * lags]
    full = windows[:, ::-1, :]
    blocks = full.reshape(2, BLOCK, lags, BLOCK).transpose(0, 2, 1, 3)
    t_re = blocks[0]
    t_im = blocks[1]
    top = jnp.concatenate([t_re, t_im], axis=2)
    bottom = jnp.concatenate([-t_im, t_re], axis=2)
    w = jnp.concatenate([top, bottom], axis=1)
    hi = lax.reduce_precision(w, exponent_bits=8, mantissa_bits=7)
    lo = (w - hi).astype(jnp.bfloat16)
    return jnp.concatenate([hi.astype(jnp.bfloat16), lo], axis=2)


def conv_kernel(x_ref, w_ref, pick_ref, o_ref, snap_ref, *, lags):
    nblocks = x_ref.shape[2] // BLOCK
    ranks = o_ref.shape[0]
    own = x_ref.shape[2] // ranks
    per_rank = own // BLOCK
    span = lags * BLOCK

    def emit(d, x_start, count):
        acc = None
        for k in range(2):
            xs = x_ref[k, :, pl.ds(x_start, count * BLOCK)]
            ws = w_ref[k, span - count * BLOCK : span]
            term = jnp.dot(xs, ws, preferred_element_type=jnp.float32)
            acc = term if acc is None else acc + term
        out = acc[:, : 2 * BLOCK] + acc[:, 2 * BLOCK :]
        rank = d // per_rank
        cols = pl.ds(pl.multiple_of((d % per_rank) * BLOCK, BLOCK), BLOCK)
        o_ref[rank, 0, :, cols] = out[:, :BLOCK].astype(o_ref.dtype)
        o_ref[rank, 1, :, cols] = out[:, BLOCK:].astype(o_ref.dtype)

    for d in range(min(lags - 1, nblocks)):
        emit(d, 0, d + 1)

    @pl.loop(lags - 1, nblocks)
    def _(d):
        emit(d, pl.multiple_of((d - (lags - 1)) * BLOCK, BLOCK), lags)

    for k in range(2):
        def gather(r, acc):
            rows = pick_ref[pl.ds(pl.multiple_of(r * own, BLOCK), own), :]
            return acc + jnp.dot(o_ref[r, k, :, :own], rows, preferred_element_type=jnp.float32)

        picked = lax.fori_loop(
            0, ranks, gather, jnp.zeros((x_ref.shape[1], TRAIN), jnp.float32)
        ).astype(o_ref.dtype)
        snap_ref[k] = picked

        @pl.loop(0, ranks)
        def _(r):
            o_ref[r, k, :, own:] = picked


def causal_filter(x, w, pick, ranks):
    _, rows, total = x.shape
    lags = w.shape[0]
    nblocks = total // BLOCK
    own = total // ranks
    flipped = w[::-1]
    stacked = jnp.stack(
        [
            flipped[:, :BLOCK].reshape(lags * BLOCK, 4 * BLOCK),
            flipped[:, BLOCK:].reshape(lags * BLOCK, 4 * BLOCK),
        ]
    )
    used = sum(min(d + 1, lags) for d in range(nblocks))
    work = 2 * rows * BLOCK * 4 * BLOCK * 2 * used + 2 * 2 * rows * total * TRAIN
    return pl.pallas_call(
        partial(conv_kernel, lags=lags),
        out_shape=(
            jax.ShapeDtypeStruct((ranks, 2, rows, own + TRAIN), jnp.bfloat16),
            jax.ShapeDtypeStruct((2, rows, TRAIN), jnp.bfloat16),
        ),
        in_specs=[pl.BlockSpec(memory_space=pltpu.VMEM)] * 3,
        out_specs=(pl.BlockSpec(memory_space=pltpu.VMEM), pl.BlockSpec(memory_space=pltpu.VMEM)),
        compiler_params=pltpu.CompilerParams(vmem_limit_bytes=48 * 1024 * 1024),
        cost_estimate=pl.CostEstimate(
            flops=work, transcendentals=0, bytes_accessed=2 * x.size * 4 + w.size * 2 + pick.size * 2
        ),
    )(x, stacked, pick)


def on_device(echoes, chirp, gates):
    chans = echoes.shape[1]
    pulses = echoes.shape[2]
    cells_dev = echoes.shape[3]
    taps = chirp.shape[1]
    ranks = lax.axis_size("range")
    range_len = cells_dev * ranks
    nblocks = range_len // BLOCK
    lags = min((taps - 1 + BLOCK - 1) // BLOCK + 1, nblocks)
    series_total = chans * pulses
    series_dev = series_total // ranks

    w = toeplitz_blocks(chirp, lags)

    local = echoes.reshape(2, series_total, cells_dev)
    x = lax.all_to_all(local, "range", split_axis=1, concat_axis=2, tiled=True)
    cells = train_cells(gates, TRAIN)
    pick = (jnp.arange(range_len, dtype=jnp.int32)[:, None] == cells[None, :]).astype(jnp.bfloat16)
    both, snap = causal_filter(x, w, pick, ranks)

    arrived = lax.all_to_all(both, "range", split_axis=0, concat_axis=0, tiled=True)
    compressed = arrived[..., :cells_dev].transpose(1, 0, 2, 3).reshape(2, chans, pulses, cells_dev)
    half = arrived[..., cells_dev:].transpose(1, 0, 2, 3).reshape(2, series_total, TRAIN)

    partner = lax.ppermute(half, "chan", [(0, 1), (1, 0)])
    upper = lax.axis_index("chan") == 0
    every = jnp.concatenate(
        [jnp.where(upper, half, partner), jnp.where(upper, partner, half)], axis=1
    )

    left = jnp.stack([snap, jnp.stack([snap[1], -snap[0]])])
    gram = lax.dot_general(
        left, every, (((1, 3), (0, 2)), ((), ())), preferred_element_type=jnp.float32
    )
    covariance = (gram * (1.0 / TRAIN)).reshape(2, 1, series_dev, -1)
    return (compressed, covariance)


def solution(mesh):
    placed = (P("groups", "chan", None, "range"), P(), P("groups", None))
    return jax.shard_map(
        on_device,
        mesh=mesh,
        in_specs=placed,
        out_specs=(P("groups", "chan", None, "range"), P("groups", "chan", "range", None)),
        check_vma=False,
    )
```
